256 devices in a mesh: dp: 16 (over x_hi, y, core), block: 16 (over z, x_lo).
Axes of the slice: x: 4 (x_hi: 2, x_lo: 2; x = x_hi * 2 + x_lo), y: 4, z: 8, core: 2. Of those that a mesh axis runs over, the one named last changes fastest.
Arguments:
- inputs: bfloat16 [128, 128, 32768], P('block', None, 'dp'), may hold values from -6 to 6
- left_factor: bfloat16 [128, 128, 128], P('block'), may hold values from -0.5 to 0.5
- right_factor: bfloat16 [128, 128, 128], P('block'), may hold values from -0.5 to 0.5
- cotangent: bfloat16 [128, 128, 32768], P('block', None, 'dp'), may hold values from -6 to 6
Outputs:
- input_grad: bfloat16 [128, 128, 32768], P('block', None, 'dp')
- left_grad: float32 [128, 128, 128], P('block', 'dp')
- right_grad: float32 [128, 128, 128], P('block', 'dp')
The draws below stay inside these ranges and needn't reach their ends.
All inputs are finite; a program needn't handle non-finite values.
Results may differ from the reference program's by a relative error of at most 0.0055.
Values may be sent and summed in bfloat16 or wider, within the bound.
No kernel may reach another device: no remote copies, remote signals or barrier semaphores. Data moves between devices by JAX's collectives and lax.ppermute only.
A program may use at most 128 MiB of HBM per device.

```python
import jax
import jax.numpy as jnp
from jax import lax

NB = 128
BS = 128
TOK_DEV = 2048
TOKENS = 32768
N_DP = 16


def block_scale(stream_key, extent, shards, low, top_value):
    factor_of = 1.0
    for axis_at, parts in shards:
        draws = jax.random.uniform(jax.random.fold_in(jax.random.fold_in(stream_key, 6), axis_at), (parts,), jnp.float32, low / len(shards), top_value / len(shards))
        factor_of = factor_of * jnp.repeat(jnp.exp(draws), extent[axis_at] // parts).reshape((-1,) + (1,) * (len(extent) - 1 - axis_at))
    return factor_of


def scatter_about(own_key, extent, scale, limit, pieces=(), kind=jnp.bfloat16):
    values = jax.random.normal(own_key, extent, jnp.float32) * scale
    if len(pieces) > 0:
        values = block_scale(own_key, extent, pieces, -0.22, 0.18) * values
    return jnp.clip(values, min=-limit, max=limit).astype(kind)


def setup_inputs(seed: int = 0) -> dict:
    splits = jax.random.split(jax.random.key(seed), 5)
    inputs = scatter_about(splits[0], (NB, BS, TOKENS), 1.0, 6.0, ((0, 16), (2, 16)))
    left_factor = scatter_about(splits[1], (NB, BS, BS), BS ** -0.5, 0.5, ((0, 16),))
    right_factor = scatter_about(splits[2], (BS, NB, NB), NB ** -0.5, 0.5, ((0, 16),))
    cotangent = scatter_about(splits[3], (BS, NB, TOKENS), 1.0, 6.0, ((0, 16), (2, 16)))
    return dict(inputs=inputs, left_factor=left_factor, right_factor=right_factor, cotangent=cotangent)


def gelu_slope(values):
    return jax.vjp(jax.nn.gelu, values)[1](jnp.ones_like(values))[0]

def reference(inputs, left_factor, right_factor, cotangent):
    left32 = left_factor.astype(jnp.float32)
    right32 = right_factor.astype(jnp.float32)
    scale = float(TOKENS) ** (-0.5)

    def step(index, carry):
        grad_input, grad_left, grad_right = carry
        start = (index * TOK_DEV).astype(jnp.int32)
        x_block = lax.dynamic_slice_in_dim(inputs, start, TOK_DEV, 2).astype(jnp.float32)
        dy_block = lax.dynamic_slice_in_dim(cotangent, start, TOK_DEV, 2)
        permuted = jnp.einsum('ict,ico->oit', x_block, left32).astype(jnp.bfloat16)
        mixed = jnp.einsum('jit,jik->jkt', permuted.astype(jnp.float32), right32)
        slope = gelu_slope(mixed)
        mixed_grad = (dy_block.astype(jnp.float32) * slope).astype(jnp.bfloat16)
        permuted_grad = jnp.einsum('jkt,jik->jit', mixed_grad.astype(jnp.float32), right32).astype(jnp.bfloat16)
        branch = jnp.einsum('oit,ico->ict', permuted_grad.astype(jnp.float32), left32)
        result = (dy_block.reshape(NB, BS, TOK_DEV).astype(jnp.float32) + branch).astype(jnp.bfloat16)
        grad_input = lax.dynamic_update_slice_in_dim(grad_input, result, start, 2)
        grad_left = grad_left + jnp.einsum('ict,oit->ico', x_block, permuted_grad.astype(jnp.float32))
        grad_right = grad_right + jnp.einsum('jit,jkt->jik', permuted.astype(jnp.float32), mixed_grad.astype(jnp.float32))
        return (grad_input, grad_left, grad_right)
    start_carry = (jnp.zeros((NB, BS, TOKENS), jnp.bfloat16), jnp.zeros((NB, BS, BS), jnp.float32), jnp.zeros((BS, NB, NB), jnp.float32))
    grad_input, grad_left, grad_right = lax.fori_loop(0, N_DP, step, start_carry)
    return (grad_input, grad_left * scale, grad_right * scale)
```

```python
import jax
import jax.numpy as jnp
from jax import lax
from jax.sharding import PartitionSpec as P

MICRO = 2


def gelu_slope(values):
    return jax.vjp(jax.nn.gelu, values)[1](jnp.ones_like(values))[0]


def dp_reduce_scatter(terms):
    n_dp = lax.axis_size("dp")
    received = lax.all_to_all(terms, "dp", split_axis=2, concat_axis=0, tiled=True)
    received = received.reshape((n_dp,) + terms.shape[:2] + (terms.shape[2] // n_dp,) + terms.shape[3:])
    return jnp.sum(received, axis=0)


def local(inputs, left_factor, right_factor, cotangent):
    tokens_local = inputs.shape[2]
    scale = float(lax.axis_size("dp") * tokens_local) ** (-0.5)
    groups = MICRO
    group_width = tokens_local // groups
    input_pieces = []
    grad_left = None
    grad_right = None
    for group in range(groups):
        x_group = inputs[:, :, group * group_width : (group + 1) * group_width]
        dy_group = cotangent[:, :, group * group_width : (group + 1) * group_width]
        outgoing = jnp.einsum(
            "ict,ico->oit", x_group, left_factor, preferred_element_type=jnp.float32
        ).astype(jnp.bfloat16)
        forward_received = lax.all_to_all(
            outgoing, "block", split_axis=0, concat_axis=1, tiled=True
        )
        mixed = jnp.einsum(
            "jit,jik->jkt", forward_received, right_factor, preferred_element_type=jnp.float32
        )
        slope = gelu_slope(mixed)
        mixed_grad = (dy_group.astype(jnp.float32) * slope).astype(jnp.bfloat16)
        right_term = (
            jnp.einsum(
                "jit,jkt->jik", forward_received, mixed_grad, preferred_element_type=jnp.float32
            )
            * scale
        )
        permuted_grad = jnp.einsum(
            "jkt,jik->jit", mixed_grad, right_factor, preferred_element_type=jnp.float32
        ).astype(jnp.bfloat16)
        received = lax.all_to_all(permuted_grad, "block", split_axis=1, concat_axis=0, tiled=True)
        branch = jnp.einsum(
            "oit,ico->ict", received, left_factor, preferred_element_type=jnp.float32
        )
        residual = dy_group.astype(jnp.float32)
        input_pieces.append((residual + branch).astype(jnp.bfloat16))
        left_term = (
            jnp.einsum("ict,oit->ico", x_group, received, preferred_element_type=jnp.float32)
            * scale
        )
        grad_left = left_term if grad_left is None else grad_left + left_term
        grad_right = right_term if grad_right is None else grad_right + right_term
    input_grad = jnp.concatenate(input_pieces, axis=2)
    reduced = dp_reduce_scatter(jnp.stack([grad_left, grad_right]))
    return (input_grad, reduced[0], reduced[1])


def solution(mesh):
    placed = (
        P("block", None, "dp"),
        P("block", None, None),
        P("block", None, None),
        P("block", None, "dp"),
    )
    return jax.shard_map(
        local,
        mesh=mesh,
        in_specs=placed,
        out_specs=(P("block", None, "dp"), P("block", "dp", None), P("block", "dp", None)),
        check_vma=False,
    )
```

```python
import jax
import jax.numpy as jnp
from jax import lax
from jax.sharding import PartitionSpec as P

CHUNKS = (3, 1)
SPLIT_DP = False


def gelu_slope(values):
    return jax.vjp(jax.nn.gelu, values)[1](jnp.ones_like(values))[0]


def dp_reduce_scatter(terms):
    n_dp = lax.axis_size("dp")
    received = lax.all_to_all(terms, "dp", split_axis=2, concat_axis=0, tiled=True)
    received = received.reshape((n_dp,) + terms.shape[:2] + (terms.shape[2] // n_dp,) + terms.shape[3:])
    return jnp.sum(received, axis=0)


def local(inputs, left_factor, right_factor, cotangent):
    tokens_local = inputs.shape[2]
    scale = float(lax.axis_size("dp") * tokens_local) ** (-0.5)
    total = sum(CHUNKS)
    bounds = [0]
    for share in CHUNKS:
        bounds.append(bounds[-1] + tokens_local * share // total)
    input_pieces = []
    grad_left = None
    grad_right = None
    right_done = None
    for group in range(len(CHUNKS)):
        lo, hi = bounds[group], bounds[group + 1]
        x_group = inputs[:, :, lo:hi]
        dy_group = cotangent[:, :, lo:hi]
        outgoing = jnp.einsum(
            "ict,ico->oit", x_group, left_factor, preferred_element_type=jnp.float32
        ).astype(jnp.bfloat16)
        forward_received = lax.all_to_all(
            outgoing, "block", split_axis=0, concat_axis=1, tiled=True
        )
        mixed = jnp.einsum(
            "jit,jik->jkt", forward_received, right_factor, preferred_element_type=jnp.float32
        )
        slope = gelu_slope(mixed)
        mixed_grad = (dy_group.astype(jnp.float32) * slope).astype(jnp.bfloat16)
        right_term = (
            jnp.einsum(
                "jit,jkt->jik", forward_received, mixed_grad, preferred_element_type=jnp.float32
            )
            * scale
        )
        grad_right = right_term if grad_right is None else grad_right + right_term
        if SPLIT_DP and group == len(CHUNKS) - 1:
            right_done = dp_reduce_scatter(grad_right[None])[0]
        permuted_grad = jnp.einsum(
            "jkt,jik->jit", mixed_grad, right_factor, preferred_element_type=jnp.float32
        ).astype(jnp.bfloat16)
        received = lax.all_to_all(permuted_grad, "block", split_axis=1, concat_axis=0, tiled=True)
        branch = jnp.einsum(
            "oit,ico->ict", received, left_factor, preferred_element_type=jnp.float32
        )
        residual = dy_group.astype(jnp.float32)
        input_pieces.append((residual + branch).astype(jnp.bfloat16))
        left_term = (
            jnp.einsum("ict,oit->ico", x_group, received, preferred_element_type=jnp.float32)
            * scale
        )
        grad_left = left_term if grad_left is None else grad_left + left_term
    input_grad = jnp.concatenate(input_pieces, axis=2)
    if SPLIT_DP:
        return (input_grad, dp_reduce_scatter(grad_left[None])[0], right_done)
    reduced = dp_reduce_scatter(jnp.stack([grad_left, grad_right]))
    return (input_grad, reduced[0], reduced[1])


def solution(mesh):
    placed = (
        P("block", None, "dp"),
        P("block", None, None),
        P("block", None, None),
        P("block", None, "dp"),
    )
    return jax.shard_map(
        local,
        mesh=mesh,
        in_specs=placed,
        out_specs=(P("block", None, "dp"), P("block", "dp", None), P("block", "dp", None)),
        check_vma=False,
    )
```

```python
import jax
import jax.numpy as jnp
from jax import lax
from jax.sharding import PartitionSpec as P

CHUNKS = (13, 3)
SPLIT_DP = False


def gelu_slope(values):
    return jax.vjp(jax.nn.gelu, values)[1](jnp.ones_like(values))[0]


def dp_reduce_scatter(terms):
    n_dp = lax.axis_size("dp")
    received = lax.all_to_all(terms, "dp", split_axis=2, concat_axis=0, tiled=True)
    received = received.reshape((n_dp,) + terms.shape[:2] + (terms.shape[2] // n_dp,) + terms.shape[3:])
    return jnp.sum(received, axis=0)


def local(inputs, left_factor, right_factor, cotangent):
    tokens_local = inputs.shape[2]
    scale = float(lax.axis_size("dp") * tokens_local) ** (-0.5)
    total = sum(CHUNKS)
    bounds = [0]
    for share in CHUNKS:
        bounds.append(bounds[-1] + tokens_local * share // total)
    input_pieces = []
    grad_left = None
    grad_right = None
    right_done = None
    for group in range(len(CHUNKS)):
        lo, hi = bounds[group], bounds[group + 1]
        x_group = inputs[:, :, lo:hi]
        dy_group = cotangent[:, :, lo:hi]
        outgoing = jnp.einsum(
            "ict,ico->oit", x_group, left_factor, preferred_element_type=jnp.float32
        ).astype(jnp.bfloat16)
        forward_received = lax.all_to_all(
            outgoing, "block", split_axis=0, concat_axis=1, tiled=True
        )
        mixed = jnp.einsum(
            "jit,jik->jkt", forward_received, right_factor, preferred_element_type=jnp.float32
        )
        slope = gelu_slope(mixed)
        mixed_grad = (dy_group.astype(jnp.float32) * slope).astype(jnp.bfloat16)
        right_term = (
            jnp.einsum(
                "jit,jkt->jik", forward_received, mixed_grad, preferred_element_type=jnp.float32
            )
            * scale
        )
        grad_right = right_term if grad_right is None else grad_right + right_term
        if SPLIT_DP and group == len(CHUNKS) - 1:
            right_done = dp_reduce_scatter(grad_right[None])[0]
        permuted_grad = jnp.einsum(
            "jkt,jik->jit", mixed_grad, right_factor, preferred_element_type=jnp.float32
        ).astype(jnp.bfloat16)
        received = lax.all_to_all(permuted_grad, "block", split_axis=1, concat_axis=0, tiled=True)
        branch = jnp.einsum(
            "oit,ico->ict", received, left_factor, preferred_element_type=jnp.float32
        )
        residual = dy_group.astype(jnp.float32)
        input_pieces.append((residual + branch).astype(jnp.bfloat16))
        left_term = (
            jnp.einsum("ict,oit->ico", x_group, received, preferred_element_type=jnp.float32)
            * scale
        )
        grad_left = left_term if grad_left is None else grad_left + left_term
    input_grad = jnp.concatenate(input_pieces, axis=2)
    if SPLIT_DP:
        return (input_grad, dp_reduce_scatter(grad_left[None])[0], right_done)
    reduced = dp_reduce_scatter(jnp.stack([grad_left, grad_right]))
    return (input_grad, reduced[0], reduced[1])


def solution(mesh):
    placed = (
        P("block", None, "dp"),
        P("block", None, None),
        P("block", None, None),
        P("block", None, "dp"),
    )
    return jax.shard_map(
        local,
        mesh=mesh,
        in_specs=placed,
        out_specs=(P("block", None, "dp"), P("block", "dp", None), P("block", "dp", None)),
        check_vma=False,
    )
```
